256 devices in a mesh: hst: 64 (over x, y, z_lo), chip: 4 (over z_hi, core).
Axes of the slice: x: 4, y: 4, z: 8 (z_hi: 2, z_lo: 4; z = z_hi * 4 + z_lo), core: 2. Of those that a mesh axis runs over, the one named last changes fastest.
Arguments:
- points: bfloat16 [131072, 1024], P(('hst', 'chip')), may hold values from -640 to 640
- assign: int32 [131072], P(('hst', 'chip')), may hold values from 0 to 8191, as said below
Outputs:
- centroids: bfloat16 [8192, 1024], P('hst', 'chip')
- nearest: float32 [131072], P(('hst', 'chip'))
The draws below stay inside these ranges and needn't reach their ends.
Inputs may be any that keep to these rules, and one draw needn't show every extreme that they name: `assign`: cluster o * 128 + j lies in owner block o. Among the 512 points of one device at most 16 name clusters of any one owner block; in every draw one owner block gets exactly 16 points from every device.
All inputs are finite; a program needn't handle non-finite values.
Results may differ from the reference program's by a relative error of at most 0.0095.
Values may be sent and summed in bfloat16 or wider, within the bound.
No kernel may reach another device: no remote copies, remote signals or barrier semaphores. Data moves between devices by JAX's collectives and lax.ppermute only.
A program may use at most 64 MiB of HBM per device.

```python
import math
import jax
import jax.numpy as jnp
from jax import lax

D = 1024
K_HOST = 128
P_DEV = 512
CYCLE = 8
K = 8192
POINTS = 131072
CAP = 16
N_HST = 64
N_CHIP = 4


def owner_table(key):
    slot_count = N_HST * CAP
    device_count = POINTS // P_DEV
    chosen = jax.random.randint(jax.random.fold_in(key, 11), (), 0, N_HST)

    def one_device(subkey):
        order_key, shuffle_key = jax.random.split(subkey)
        ordering = jax.random.permutation(order_key, slot_count)
        slot_owner = ordering // CAP
        ranking = jnp.where(slot_owner == chosen, 0, slot_count) + jnp.arange(slot_count)
        picked = slot_owner[jnp.argsort(ranking)[:P_DEV]]
        return picked[jax.random.permutation(shuffle_key, P_DEV)]
    device_keys = jax.random.split(jax.random.fold_in(key, 12), device_count)
    owners_all = jax.vmap(one_device)(device_keys).reshape(POINTS)
    within = jax.random.randint(jax.random.fold_in(key, 13), (POINTS,), 0, K_HOST)
    return (owners_all * K_HOST + within).astype(jnp.int32)


def draw_assign(key, part):
    return owner_table(key)


def draw_points(key, part):
    labels = owner_table(key)
    centres = jax.random.truncated_normal(jax.random.fold_in(key, 21), -4.0, 4.0, (K, D), jnp.float32)
    noise = jax.random.truncated_normal(jax.random.fold_in(key, 22), -4.0, 4.0, (POINTS, D), jnp.float32)
    column_scale = jnp.exp(jax.random.uniform(jax.random.fold_in(key, 23), (D,), jnp.float32, 0.0, math.log(10.0)))
    values = (1.5 * centres[labels] + noise) * column_scale[None, :]
    return values.astype(jnp.bfloat16)


def setup_inputs(seed: int = 0) -> dict:
    key_of = jax.random.split(jax.random.key(seed), 3)
    return {
        "points": draw_points(jax.random.fold_in(key_of[2], 71), 0),
        "assign": draw_assign(jax.random.fold_in(key_of[2], 71), 0),
    }


EPSILON = 1e-06

def reference(points, assign):
    host_rows = N_CHIP * P_DEV
    pieces = points.reshape(N_HST, host_rows, D)
    labels = assign.reshape(N_HST, host_rows)

    def add_host(running, item):
        values, groups = item
        return (running + jax.ops.segment_sum(values.astype(jnp.float32), groups, num_segments=K), None)
    sums, unused = lax.scan(add_host, jnp.zeros((K, D), jnp.float32), (pieces, labels))
    factor = lax.rsqrt(lax.optimization_barrier(jnp.mean(sums * sums, axis=1, keepdims=True)) + EPSILON)
    centroids = (sums * factor).astype(jnp.bfloat16)
    blocks = centroids.reshape(N_HST, K_HOST, D)

    def host_nearest(host_index):
        widened = pieces[host_index].astype(jnp.float32)
        unit_points = (widened * lax.rsqrt(lax.optimization_barrier(jnp.mean(widened * widened, axis=1, keepdims=True)) + EPSILON)).astype(jnp.bfloat16)
        chosen = (host_index - jnp.arange(CYCLE, dtype=jnp.int32)) % N_HST
        window = blocks[chosen].reshape(CYCLE * K_HOST, D)
        scores = jnp.einsum('pd,kd->pk', unit_points.astype(jnp.float32), window.astype(jnp.float32))
        return lax.optimization_barrier(jnp.min(2.0 - 2.0 * scores / D, axis=1))
    nearest = lax.map(host_nearest, jnp.arange(N_HST, dtype=jnp.int32)).reshape(POINTS)
    return (centroids, nearest)
```

```python
import jax
import jax.numpy as jnp
from jax import lax
from jax.sharding import PartitionSpec as P

K_HOST = 128
CYCLE = 8
CAP = 16
LABEL_LANES = 128

EPSILON = 1e-06


def shifted(block, axis, distance):
    devices = range(lax.axis_size(axis))
    route = [((i - distance) % len(devices), i) for i in devices]
    return lax.ppermute(block, axis, route)


def pack_by_owner(points, assign, owner_count):
    row_count = points.shape[0]
    owner = assign // K_HOST
    local = assign % K_HOST
    index = jnp.arange(row_count, dtype=jnp.int32)
    earlier = (owner[:, None] == owner[None, :]) & (index[None, :] < index[:, None])
    rank = jnp.sum(earlier.astype(jnp.int32), axis=1)
    slot = owner * CAP + rank
    slots = jnp.arange(owner_count * CAP, dtype=jnp.int32)
    select = (slots[:, None] == slot[None, :]).astype(jnp.bfloat16)
    tag = jnp.broadcast_to((local + 1).astype(jnp.bfloat16)[:, None], (row_count, LABEL_LANES))
    widened = jnp.concatenate([points, tag], axis=1)
    return jnp.dot(select, widened, preferred_element_type=jnp.float32).astype(jnp.bfloat16)


def body(points, assign):
    feature_count = points.shape[1]
    owner_count = lax.axis_size("hst")
    chip_index = lax.axis_index("chip")
    quarter = feature_count // lax.axis_size("chip")

    packed = pack_by_owner(points, assign, owner_count)
    arrived = lax.all_to_all(packed, "hst", 0, 0, tiled=True)
    rows = arrived[:, :feature_count]
    labels = arrived[:, feature_count].astype(jnp.int32) - 1
    clusters = jnp.arange(K_HOST, dtype=jnp.int32)
    member = (clusters[:, None] == labels[None, :]).astype(jnp.bfloat16)
    partial = jnp.dot(member, rows, preferred_element_type=jnp.float32)
    sums = lax.psum(partial, "chip")
    factor = lax.rsqrt(jnp.mean(sums * sums, axis=1, keepdims=True) + EPSILON)
    own_block = (sums * factor).astype(jnp.bfloat16)
    centroids = lax.dynamic_slice_in_dim(own_block, chip_index * quarter, quarter, 1)

    widened = points.astype(jnp.float32)
    unit_points = (
        widened * lax.rsqrt(jnp.mean(widened * widened, axis=1, keepdims=True) + EPSILON)
    ).astype(jnp.bfloat16)

    def nearest_in(candidates):
        scores = jnp.einsum(
            "pd,kd->pk", unit_points, candidates, preferred_element_type=jnp.float32
        )
        return jnp.min(2.0 - 2.0 * scores / feature_count, axis=1)

    nearest = nearest_in(own_block)
    for distance in range(1, CYCLE):
        nearest = jnp.minimum(nearest, nearest_in(shifted(own_block, "hst", distance)))
    return (centroids, nearest)


def solution(mesh):
    in_specs = (P(("hst", "chip"), None), P(("hst", "chip")))
    out_specs = (P("hst", "chip"), P(("hst", "chip")))
    return jax.shard_map(body, mesh=mesh, in_specs=in_specs, out_specs=out_specs, check_vma=False)
```

```python
import jax
import jax.numpy as jnp
from jax import lax
from jax.sharding import PartitionSpec as P

K_HOST = 128
CYCLE = 8
CAP = 16
LABEL_LANES = 128

EPSILON = 1e-06


def shifted(block, axis, distance):
    devices = range(lax.axis_size(axis))
    route = [((i - distance) % len(devices), i) for i in devices]
    return lax.ppermute(block, axis, route)


def swapped(block, axis, mask):
    return lax.ppermute(block, axis, [(i, i ^ mask) for i in range(lax.axis_size(axis))])


def pack_by_owner(points, assign, owner_count):
    row_count = points.shape[0]
    owner = assign // K_HOST
    local = assign % K_HOST
    index = jnp.arange(row_count, dtype=jnp.int32)
    earlier = (owner[:, None] == owner[None, :]) & (index[None, :] < index[:, None])
    rank = jnp.sum(earlier.astype(jnp.int32), axis=1)
    slot = owner * CAP + rank
    slots = jnp.arange(owner_count * CAP, dtype=jnp.int32)
    select = (slots[:, None] == slot[None, :]).astype(jnp.bfloat16)
    tag = jnp.broadcast_to((local + 1).astype(jnp.bfloat16)[:, None], (row_count, LABEL_LANES))
    widened = jnp.concatenate([points, tag], axis=1)
    return jnp.dot(select, widened, preferred_element_type=jnp.float32).astype(jnp.bfloat16)


def body(points, assign):
    feature_count = points.shape[1]
    owner_count = lax.axis_size("hst")
    chip_index = lax.axis_index("chip")
    quarter = feature_count // lax.axis_size("chip")
    half = feature_count // 2
    core = chip_index % 2

    packed = pack_by_owner(points, assign, owner_count)
    arrived = lax.all_to_all(packed, "hst", 0, 0, tiled=True)
    rows = arrived[:, :feature_count]
    labels = arrived[:, feature_count].astype(jnp.int32) - 1
    clusters = jnp.arange(K_HOST, dtype=jnp.int32)
    member = (clusters[:, None] == labels[None, :]).astype(jnp.bfloat16)
    partial = jnp.dot(member, rows, preferred_element_type=jnp.float32)

    keep = lax.dynamic_slice_in_dim(partial, core * half, half, 1)
    give = lax.dynamic_slice_in_dim(partial, (1 - core) * half, half, 1)
    pair = keep + swapped(give, "chip", 1)
    mine = pair + swapped(pair, "chip", 2)
    other = swapped(mine, "chip", 1)
    sums = jnp.where(
        core == 0,
        jnp.concatenate([mine, other], axis=1),
        jnp.concatenate([other, mine], axis=1),
    )
    factor = lax.rsqrt(jnp.mean(sums * sums, axis=1, keepdims=True) + EPSILON)
    own_block = (sums * factor).astype(jnp.bfloat16)
    centroids = lax.dynamic_slice_in_dim(own_block, chip_index * quarter, quarter, 1)

    widened = points.astype(jnp.float32)
    unit_points = (
        widened * lax.rsqrt(jnp.mean(widened * widened, axis=1, keepdims=True) + EPSILON)
    ).astype(jnp.bfloat16)
    unit_mine = lax.dynamic_slice_in_dim(unit_points, core * half, half, 1)
    unit_other = lax.dynamic_slice_in_dim(unit_points, (1 - core) * half, half, 1)

    def nearest_in(candidates_mine, candidates_other):
        scores = jnp.einsum(
            "pd,kd->pk", unit_mine, candidates_mine, preferred_element_type=jnp.float32
        ) + jnp.einsum(
            "pd,kd->pk", unit_other, candidates_other, preferred_element_type=jnp.float32
        )
        return jnp.min(2.0 - 2.0 * scores / feature_count, axis=1)

    own_mine = lax.dynamic_slice_in_dim(own_block, core * half, half, 1)
    own_other = lax.dynamic_slice_in_dim(own_block, (1 - core) * half, half, 1)
    nearest = nearest_in(own_mine, own_other)
    for distance in range(1, CYCLE):
        moved = shifted(own_mine, "hst", distance)
        nearest = jnp.minimum(nearest, nearest_in(moved, swapped(moved, "chip", 1)))
    return (centroids, nearest)


def solution(mesh):
    in_specs = (P(("hst", "chip"), None), P(("hst", "chip")))
    out_specs = (P("hst", "chip"), P(("hst", "chip")))
    return jax.shard_map(body, mesh=mesh, in_specs=in_specs, out_specs=out_specs, check_vma=False)
```

```python
import jax
import jax.numpy as jnp
from jax import lax
from jax.sharding import PartitionSpec as P

K_HOST = 128
CYCLE = 8
CAP = 16
LABEL_LANES = 128

EPSILON = 1e-06


def shifted(block, axis, distance):
    devices = range(lax.axis_size(axis))
    route = [((i - distance) % len(devices), i) for i in devices]
    return lax.ppermute(block, axis, route)


def swapped(block, axis, mask):
    return lax.ppermute(block, axis, [(i, i ^ mask) for i in range(lax.axis_size(axis))])


def pack_by_owner(points, assign, owner_count):
    row_count = points.shape[0]
    owner = assign // K_HOST
    local = assign % K_HOST
    index = jnp.arange(row_count, dtype=jnp.int32)
    earlier = (owner[:, None] == owner[None, :]) & (index[None, :] < index[:, None])
    rank = jnp.sum(earlier.astype(jnp.int32), axis=1)
    slot = owner * CAP + rank
    slots = jnp.arange(owner_count * CAP, dtype=jnp.int32)
    select = (slots[:, None] == slot[None, :]).astype(jnp.bfloat16)
    source = jnp.sum(select.astype(jnp.int32) * index[None, :], axis=1)
    filled = jnp.sum(select.astype(jnp.int32), axis=1) > 0
    tag = jnp.where(filled, local[source] + 1, 0).astype(jnp.bfloat16)
    flat = points[source].reshape(owner_count, CAP * points.shape[1])
    tags = jnp.pad(tag.reshape(owner_count, CAP), ((0, 0), (0, LABEL_LANES - CAP)))
    return jnp.concatenate([flat, tags], axis=1)


def body(points, assign):
    feature_count = points.shape[1]
    owner_count = lax.axis_size("hst")
    chip_index = lax.axis_index("chip")
    quarter = feature_count // lax.axis_size("chip")
    half = feature_count // 2
    core = chip_index % 2

    packed = pack_by_owner(points, assign, owner_count)
    arrived = lax.all_to_all(packed, "hst", 0, 0, tiled=True)
    rows = arrived[:, : CAP * feature_count].reshape(owner_count * CAP, feature_count)
    labels = arrived[:, CAP * feature_count : CAP * feature_count + CAP].reshape(-1)
    labels = labels.astype(jnp.int32) - 1
    clusters = jnp.arange(K_HOST, dtype=jnp.int32)
    member = (clusters[:, None] == labels[None, :]).astype(jnp.bfloat16)
    partial = jnp.dot(member, rows, preferred_element_type=jnp.float32)

    keep = lax.dynamic_slice_in_dim(partial, core * half, half, 1)
    give = lax.dynamic_slice_in_dim(partial, (1 - core) * half, half, 1)
    pair = keep + swapped(give, "chip", 1)
    mine = pair + swapped(pair, "chip", 2)
    other = swapped(mine, "chip", 1)
    sums = jnp.where(
        core == 0,
        jnp.concatenate([mine, other], axis=1),
        jnp.concatenate([other, mine], axis=1),
    )
    factor = lax.rsqrt(jnp.mean(sums * sums, axis=1, keepdims=True) + EPSILON)
    own_block = (sums * factor).astype(jnp.bfloat16)
    centroids = lax.dynamic_slice_in_dim(own_block, chip_index * quarter, quarter, 1)

    widened = points.astype(jnp.float32)
    unit_points = (
        widened * lax.rsqrt(jnp.mean(widened * widened, axis=1, keepdims=True) + EPSILON)
    ).astype(jnp.bfloat16)
    unit_mine = lax.dynamic_slice_in_dim(unit_points, core * half, half, 1)
    unit_other = lax.dynamic_slice_in_dim(unit_points, (1 - core) * half, half, 1)

    def nearest_in(candidates_mine, candidates_other):
        scores = jnp.einsum(
            "pd,kd->pk", unit_mine, candidates_mine, preferred_element_type=jnp.float32
        ) + jnp.einsum(
            "pd,kd->pk", unit_other, candidates_other, preferred_element_type=jnp.float32
        )
        return jnp.min(2.0 - 2.0 * scores / feature_count, axis=1)

    own_mine = lax.dynamic_slice_in_dim(own_block, core * half, half, 1)
    own_other = lax.dynamic_slice_in_dim(own_block, (1 - core) * half, half, 1)
    nearest = nearest_in(own_mine, own_other)
    for distance in range(1, CYCLE):
        moved = shifted(own_mine, "hst", distance)
        nearest = jnp.minimum(nearest, nearest_in(moved, swapped(moved, "chip", 1)))
    return (centroids, nearest)


def solution(mesh):
    in_specs = (P(("hst", "chip"), None), P(("hst", "chip")))
    out_specs = (P("hst", "chip"), P(("hst", "chip")))
    return jax.shard_map(body, mesh=mesh, in_specs=in_specs, out_specs=out_specs, check_vma=False)
```

```python
import jax
import jax.numpy as jnp
from jax import lax
from jax.sharding import PartitionSpec as P

K_HOST = 128
CYCLE = 8
CAP = 16
LABEL_LANES = 128

EPSILON = 1e-06


def shifted(block, axis, distance):
    devices = range(lax.axis_size(axis))
    route = [((i - distance) % len(devices), i) for i in devices]
    return lax.ppermute(block, axis, route)


def window_route(hst_count, chip_count, distance):
    route = []
    for h in range(hst_count):
        s = (h - distance) % hst_count
        gap = abs(h % 4 - s % 4)
        for c in range(chip_count):
            half, core = divmod(c, 2)
            flip = 1 if gap == 3 or (gap == 2 and core == 1) else 0
            route.append((s * chip_count + (half ^ flip) * 2 + core, h * chip_count + c))
    return route


def swapped(block, axis, mask):
    return lax.ppermute(block, axis, [(i, i ^ mask) for i in range(lax.axis_size(axis))])


def pack_by_owner(points, assign, owner_count):
    row_count = points.shape[0]
    owner = assign // K_HOST
    local = assign % K_HOST
    index = jnp.arange(row_count, dtype=jnp.int32)
    earlier = (owner[:, None] == owner[None, :]) & (index[None, :] < index[:, None])
    rank = jnp.sum(earlier.astype(jnp.int32), axis=1)
    slot = owner * CAP + rank
    slots = jnp.arange(owner_count * CAP, dtype=jnp.int32)
    select = (slots[:, None] == slot[None, :]).astype(jnp.bfloat16)
    tag = jnp.broadcast_to((local + 1).astype(jnp.bfloat16)[:, None], (row_count, LABEL_LANES))
    widened = jnp.concatenate([points, tag], axis=1)
    return jnp.dot(select, widened, preferred_element_type=jnp.float32).astype(jnp.bfloat16)


def body(points, assign):
    feature_count = points.shape[1]
    owner_count = lax.axis_size("hst")
    chip_index = lax.axis_index("chip")
    quarter = feature_count // lax.axis_size("chip")
    half = feature_count // 2
    core = chip_index % 2

    packed = pack_by_owner(points, assign, owner_count)
    arrived = lax.all_to_all(packed, "hst", 0, 0, tiled=True)
    rows = arrived[:, :feature_count]
    labels = arrived[:, feature_count].astype(jnp.int32) - 1
    clusters = jnp.arange(K_HOST, dtype=jnp.int32)
    member = (clusters[:, None] == labels[None, :]).astype(jnp.bfloat16)
    partial = jnp.dot(member, rows, preferred_element_type=jnp.float32)

    keep = lax.dynamic_slice_in_dim(partial, core * half, half, 1)
    give = lax.dynamic_slice_in_dim(partial, (1 - core) * half, half, 1)
    pair = keep + swapped(give, "chip", 1)
    mine = pair + swapped(pair, "chip", 2)
    other = swapped(mine, "chip", 1)
    sums = jnp.where(
        core == 0,
        jnp.concatenate([mine, other], axis=1),
        jnp.concatenate([other, mine], axis=1),
    )
    factor = lax.rsqrt(jnp.mean(sums * sums, axis=1, keepdims=True) + EPSILON)
    own_block = (sums * factor).astype(jnp.bfloat16)
    centroids = lax.dynamic_slice_in_dim(own_block, chip_index * quarter, quarter, 1)

    widened = points.astype(jnp.float32)
    unit_points = (
        widened * lax.rsqrt(jnp.mean(widened * widened, axis=1, keepdims=True) + EPSILON)
    ).astype(jnp.bfloat16)
    unit_mine = lax.dynamic_slice_in_dim(unit_points, core * half, half, 1)
    unit_other = lax.dynamic_slice_in_dim(unit_points, (1 - core) * half, half, 1)

    def nearest_in(candidates_mine, candidates_other):
        scores = jnp.einsum(
            "pd,kd->pk", unit_mine, candidates_mine, preferred_element_type=jnp.float32
        ) + jnp.einsum(
            "pd,kd->pk", unit_other, candidates_other, preferred_element_type=jnp.float32
        )
        return jnp.min(2.0 - 2.0 * scores / feature_count, axis=1)

    own_mine = lax.dynamic_slice_in_dim(own_block, core * half, half, 1)
    own_other = lax.dynamic_slice_in_dim(own_block, (1 - core) * half, half, 1)
    nearest = nearest_in(own_mine, own_other)
    for distance in range(1, CYCLE):
        moved = lax.ppermute(
            own_mine, ("hst", "chip"), window_route(owner_count, lax.axis_size("chip"), distance)
        )
        nearest = jnp.minimum(nearest, nearest_in(moved, swapped(moved, "chip", 1)))
    return (centroids, nearest)


def solution(mesh):
    in_specs = (P(("hst", "chip"), None), P(("hst", "chip")))
    out_specs = (P("hst", "chip"), P(("hst", "chip")))
    return jax.shard_map(body, mesh=mesh, in_specs=in_specs, out_specs=out_specs, check_vma=False)
```

```python
import jax
import jax.numpy as jnp
from jax import lax
from jax.sharding import PartitionSpec as P

K_HOST = 128
CYCLE = 8
CAP = 16
LABEL_LANES = 128

EPSILON = 1e-06


def shifted(block, axis, distance):
    devices = range(lax.axis_size(axis))
    route = [((i - distance) % len(devices), i) for i in devices]
    return lax.ppermute(block, axis, route)


def window_route(hst_count, chip_count, reach):
    route = []
    for h in range(hst_count):
        for c in range(chip_count):
            half, core = divmod(c, 2)
            if reach[core] is None:
                continue
            s = (h - reach[core]) % hst_count
            gap = abs(h % 4 - s % 4)
            flip = 1 if gap == 3 or (gap == 2 and core == 1) else 0
            route.append((s * chip_count + (half ^ flip) * 2 + core, h * chip_count + c))
    return route


def swapped(block, axis, mask):
    return lax.ppermute(block, axis, [(i, i ^ mask) for i in range(lax.axis_size(axis))])


def pack_by_owner(points, assign, owner_count):
    row_count = points.shape[0]
    owner = assign // K_HOST
    local = assign % K_HOST
    index = jnp.arange(row_count, dtype=jnp.int32)
    earlier = (owner[:, None] == owner[None, :]) & (index[None, :] < index[:, None])
    rank = jnp.sum(earlier.astype(jnp.int32), axis=1)
    slot = owner * CAP + rank
    slots = jnp.arange(owner_count * CAP, dtype=jnp.int32)
    select = (slots[:, None] == slot[None, :]).astype(jnp.bfloat16)
    tag = jnp.broadcast_to((local + 1).astype(jnp.bfloat16)[:, None], (row_count, LABEL_LANES))
    widened = jnp.concatenate([points, tag], axis=1)
    return jnp.dot(select, widened, preferred_element_type=jnp.float32).astype(jnp.bfloat16)


def body(points, assign):
    feature_count = points.shape[1]
    owner_count = lax.axis_size("hst")
    chip_index = lax.axis_index("chip")
    quarter = feature_count // lax.axis_size("chip")
    half = feature_count // 2
    core = chip_index % 2

    packed = pack_by_owner(points, assign, owner_count)
    arrived = lax.all_to_all(packed, "hst", 0, 0, tiled=True)
    rows = arrived[:, :feature_count]
    labels = arrived[:, feature_count].astype(jnp.int32) - 1
    clusters = jnp.arange(K_HOST, dtype=jnp.int32)
    member = (clusters[:, None] == labels[None, :]).astype(jnp.bfloat16)
    partial = jnp.dot(member, rows, preferred_element_type=jnp.float32)

    keep = lax.dynamic_slice_in_dim(partial, core * half, half, 1)
    give = lax.dynamic_slice_in_dim(partial, (1 - core) * half, half, 1)
    pair = keep + swapped(give, "chip", 1)
    mine = pair + swapped(pair, "chip", 2)
    other = swapped(mine, "chip", 1)
    sums = jnp.where(
        core == 0,
        jnp.concatenate([mine, other], axis=1),
        jnp.concatenate([other, mine], axis=1),
    )
    factor = lax.rsqrt(jnp.mean(sums * sums, axis=1, keepdims=True) + EPSILON)
    own_block = (sums * factor).astype(jnp.bfloat16)
    centroids = lax.dynamic_slice_in_dim(own_block, chip_index * quarter, quarter, 1)

    widened = points.astype(jnp.float32)
    unit_points = (
        widened * lax.rsqrt(jnp.mean(widened * widened, axis=1, keepdims=True) + EPSILON)
    ).astype(jnp.bfloat16)
    unit_partner = swapped(unit_points, "chip", 1)

    def nearest_in(unit, candidates):
        scores = jnp.einsum("pd,kd->pk", unit, candidates, preferred_element_type=jnp.float32)
        return jnp.min(2.0 - 2.0 * scores / feature_count, axis=1)

    half_cycle = CYCLE // 2
    fetched = [
        lax.ppermute(
            own_block,
            ("hst", "chip"),
            window_route(
                owner_count,
                lax.axis_size("chip"),
                (step if step < half_cycle else None, half_cycle - 1 + step),
            ),
        )
        for step in range(1, half_cycle + 1)
    ]
    blocks = [jnp.where(core == 0, own_block, fetched[-1])] + fetched[:-1]
    nearest = nearest_in(unit_points, blocks[0])
    partner_nearest = nearest_in(unit_partner, blocks[0])
    for block in blocks[1:]:
        nearest = jnp.minimum(nearest, nearest_in(unit_points, block))
        partner_nearest = jnp.minimum(partner_nearest, nearest_in(unit_partner, block))
    nearest = jnp.minimum(nearest, swapped(partner_nearest, "chip", 1))
    return (centroids, nearest)


def solution(mesh):
    in_specs = (P(("hst", "chip"), None), P(("hst", "chip")))
    out_specs = (P("hst", "chip"), P(("hst", "chip")))
    return jax.shard_map(body, mesh=mesh, in_specs=in_specs, out_specs=out_specs, check_vma=False)
```

```python
import jax
import jax.numpy as jnp
from jax import lax
from jax.sharding import PartitionSpec as P

K_HOST = 128
CYCLE = 8
CAP = 16

EPSILON = 1e-06


def shifted(block, axis, distance):
    devices = range(lax.axis_size(axis))
    route = [((i - distance) % len(devices), i) for i in devices]
    return lax.ppermute(block, axis, route)


def window_route(hst_count, chip_count, reach):
    route = []
    for h in range(hst_count):
        for c in range(chip_count):
            half, core = divmod(c, 2)
            if reach[core] is None:
                continue
            s = (h - reach[core]) % hst_count
            gap = abs(h % 4 - s % 4)
            flip = 1 if gap == 3 or (gap == 2 and core == 1) else 0
            route.append((s * chip_count + (half ^ flip) * 2 + core, h * chip_count + c))
    return route


def swapped(block, axis, mask):
    return lax.ppermute(block, axis, [(i, i ^ mask) for i in range(lax.axis_size(axis))])


def pack_by_owner(points, assign, owner_count):
    row_count = points.shape[0]
    owner = assign // K_HOST
    local = assign % K_HOST
    index = jnp.arange(row_count, dtype=jnp.int32)
    earlier = (owner[:, None] == owner[None, :]) & (index[None, :] < index[:, None])
    rank = jnp.sum(earlier.astype(jnp.int32), axis=1)
    slot = owner * CAP + rank
    slots = jnp.arange(owner_count * CAP, dtype=jnp.int32)
    select = (slots[:, None] == slot[None, :]).astype(jnp.bfloat16)
    return jnp.dot(select, points, preferred_element_type=jnp.float32).astype(jnp.bfloat16)


def slot_labels(every_assign, owner):
    mine = (every_assign // K_HOST) == owner
    rank = jnp.cumsum(mine.astype(jnp.int32), axis=1) - mine.astype(jnp.int32)
    slot = jnp.arange(CAP, dtype=jnp.int32)
    hit = mine[:, None, :] & (rank[:, None, :] == slot[None, :, None])
    local = (every_assign % K_HOST + 1)[:, None, :]
    return (jnp.sum(jnp.where(hit, local, 0), axis=2) - 1).reshape(-1)


def body(points, assign):
    feature_count = points.shape[1]
    owner_count = lax.axis_size("hst")
    chip_index = lax.axis_index("chip")
    quarter = feature_count // lax.axis_size("chip")
    half = feature_count // 2
    core = chip_index % 2

    every_assign = lax.all_gather(assign, "hst", axis=0)
    packed = pack_by_owner(points, assign, owner_count)
    rows = lax.all_to_all(packed, "hst", 0, 0, tiled=True)
    labels = slot_labels(every_assign, lax.axis_index("hst"))
    clusters = jnp.arange(K_HOST, dtype=jnp.int32)
    member = (clusters[:, None] == labels[None, :]).astype(jnp.bfloat16)
    partial = jnp.dot(member, rows, preferred_element_type=jnp.float32)

    keep = lax.dynamic_slice_in_dim(partial, core * half, half, 1)
    give = lax.dynamic_slice_in_dim(partial, (1 - core) * half, half, 1)
    pair = keep + swapped(give, "chip", 1)
    mine = pair + swapped(pair, "chip", 2)
    other = swapped(mine, "chip", 1)
    sums = jnp.where(
        core == 0,
        jnp.concatenate([mine, other], axis=1),
        jnp.concatenate([other, mine], axis=1),
    )
    factor = lax.rsqrt(jnp.mean(sums * sums, axis=1, keepdims=True) + EPSILON)
    own_block = (sums * factor).astype(jnp.bfloat16)
    centroids = lax.dynamic_slice_in_dim(own_block, chip_index * quarter, quarter, 1)

    widened = points.astype(jnp.float32)
    unit_points = (
        widened * lax.rsqrt(jnp.mean(widened * widened, axis=1, keepdims=True) + EPSILON)
    ).astype(jnp.bfloat16)
    unit_partner = swapped(unit_points, "chip", 1)

    def nearest_in(unit, candidates):
        scores = jnp.einsum("pd,kd->pk", unit, candidates, preferred_element_type=jnp.float32)
        return jnp.min(2.0 - 2.0 * scores / feature_count, axis=1)

    half_cycle = CYCLE // 2
    fetched = [
        lax.ppermute(
            own_block,
            ("hst", "chip"),
            window_route(
                owner_count,
                lax.axis_size("chip"),
                (step if step < half_cycle else None, half_cycle - 1 + step),
            ),
        )
        for step in range(1, half_cycle + 1)
    ]
    blocks = [jnp.where(core == 0, own_block, fetched[-1])] + fetched[:-1]
    nearest = nearest_in(unit_points, blocks[0])
    partner_nearest = nearest_in(unit_partner, blocks[0])
    for block in blocks[1:]:
        nearest = jnp.minimum(nearest, nearest_in(unit_points, block))
        partner_nearest = jnp.minimum(partner_nearest, nearest_in(unit_partner, block))
    nearest = jnp.minimum(nearest, swapped(partner_nearest, "chip", 1))
    return (centroids, nearest)


def solution(mesh):
    in_specs = (P(("hst", "chip"), None), P(("hst", "chip")))
    out_specs = (P("hst", "chip"), P(("hst", "chip")))
    return jax.shard_map(body, mesh=mesh, in_specs=in_specs, out_specs=out_specs, check_vma=False)
```

```python
import jax
import jax.numpy as jnp
from jax import lax
from jax.sharding import PartitionSpec as P

K_HOST = 128
CYCLE = 8
CAP = 16
LABEL_LANES = 128

EPSILON = 1e-06


def shifted(block, axis, distance):
    devices = range(lax.axis_size(axis))
    route = [((i - distance) % len(devices), i) for i in devices]
    return lax.ppermute(block, axis, route)


def window_route(hst_count, chip_count, reach):
    route = []
    for h in range(hst_count):
        for c in range(chip_count):
            half, core = divmod(c, 2)
            if reach[core] is None:
                continue
            s = (h - reach[core]) % hst_count
            gap = abs(h % 4 - s % 4)
            flip = 1 if gap == 3 or (gap == 2 and core == 1) else 0
            route.append((s * chip_count + (half ^ flip) * 2 + core, h * chip_count + c))
    return route


def swapped(block, axis, mask):
    return lax.ppermute(block, axis, [(i, i ^ mask) for i in range(lax.axis_size(axis))])


def pack_by_owner(points, assign, owner_count):
    row_count = points.shape[0]
    owner = assign // K_HOST
    local = assign % K_HOST
    index = jnp.arange(row_count, dtype=jnp.int32)
    earlier = (owner[:, None] == owner[None, :]) & (index[None, :] < index[:, None])
    rank = jnp.sum(earlier.astype(jnp.int32), axis=1)
    slot = owner * CAP + rank
    slots = jnp.arange(owner_count * CAP, dtype=jnp.int32)
    select = (slots[:, None] == slot[None, :]).astype(jnp.bfloat16)
    tag = jnp.broadcast_to((local + 1).astype(jnp.bfloat16)[:, None], (row_count, LABEL_LANES))
    widened = jnp.concatenate([points, tag], axis=1)
    return jnp.dot(select, widened, preferred_element_type=jnp.float32).astype(jnp.bfloat16)


def body(points, assign):
    feature_count = points.shape[1]
    owner_count = lax.axis_size("hst")
    chip_index = lax.axis_index("chip")
    quarter = feature_count // lax.axis_size("chip")
    half = feature_count // 2
    core = chip_index % 2

    packed = pack_by_owner(points, assign, owner_count)
    arrived = lax.all_to_all(packed, "hst", 0, 0, tiled=True)
    rows = arrived[:, :feature_count]
    labels = arrived[:, feature_count].astype(jnp.int32) - 1
    clusters = jnp.arange(K_HOST, dtype=jnp.int32)
    member = (clusters[:, None] == labels[None, :]).astype(jnp.bfloat16)
    partial = jnp.dot(member, rows, preferred_element_type=jnp.float32)

    chunk_count = 2
    chunk = K_HOST // chunk_count
    own_chunks = []
    for part in range(chunk_count):
        piece = partial[part * chunk : (part + 1) * chunk]
        keep = lax.dynamic_slice_in_dim(piece, core * half, half, 1)
        give = lax.dynamic_slice_in_dim(piece, (1 - core) * half, half, 1)
        pair = keep + swapped(give, "chip", 1)
        mine = pair + swapped(pair, "chip", 2)
        other = swapped(mine, "chip", 1)
        sums = jnp.where(
            core == 0,
            jnp.concatenate([mine, other], axis=1),
            jnp.concatenate([other, mine], axis=1),
        )
        factor = lax.rsqrt(jnp.mean(sums * sums, axis=1, keepdims=True) + EPSILON)
        own_chunks.append((sums * factor).astype(jnp.bfloat16))
    centroids = jnp.concatenate(
        [lax.dynamic_slice_in_dim(c, chip_index * quarter, quarter, 1) for c in own_chunks], axis=0
    )

    widened = points.astype(jnp.float32)
    unit_points = (
        widened * lax.rsqrt(jnp.mean(widened * widened, axis=1, keepdims=True) + EPSILON)
    ).astype(jnp.bfloat16)
    unit_partner = swapped(unit_points, "chip", 1)

    def nearest_in(unit, candidates):
        scores = jnp.einsum("pd,kd->pk", unit, candidates, preferred_element_type=jnp.float32)
        return jnp.min(2.0 - 2.0 * scores / feature_count, axis=1)

    half_cycle = CYCLE // 2
    nearest = None
    for own_block in own_chunks:
        fetched = [
            lax.ppermute(
                own_block,
                ("hst", "chip"),
                window_route(
                    owner_count,
                    lax.axis_size("chip"),
                    (step if step < half_cycle else None, half_cycle - 1 + step),
                ),
            )
            for step in range(1, half_cycle + 1)
        ]
        blocks = [jnp.where(core == 0, own_block, fetched[-1])] + fetched[:-1]
        for block in blocks:
            found = nearest_in(unit_points, block)
            partner_found = nearest_in(unit_partner, block)
            if nearest is None:
                nearest, partner_nearest = found, partner_found
            else:
                nearest = jnp.minimum(nearest, found)
                partner_nearest = jnp.minimum(partner_nearest, partner_found)
    nearest = jnp.minimum(nearest, swapped(partner_nearest, "chip", 1))
    return (centroids, nearest)


def solution(mesh):
    in_specs = (P(("hst", "chip"), None), P(("hst", "chip")))
    out_specs = (P("hst", "chip"), P(("hst", "chip")))
    return jax.shard_map(body, mesh=mesh, in_specs=in_specs, out_specs=out_specs, check_vma=False)
```

```python
import jax
import jax.numpy as jnp
from jax import lax
from jax.sharding import PartitionSpec as P

K_HOST = 128
CYCLE = 8
CAP = 16
LABEL_LANES = 128

EPSILON = 1e-06


def shifted(block, axis, distance):
    devices = range(lax.axis_size(axis))
    route = [((i - distance) % len(devices), i) for i in devices]
    return lax.ppermute(block, axis, route)


def window_route(hst_count, chip_count, reach):
    route = []
    for h in range(hst_count):
        for c in range(chip_count):
            half, core = divmod(c, 2)
            if reach[core] is None:
                continue
            s = (h - reach[core]) % hst_count
            gap = abs(h % 4 - s % 4)
            flip = 1 if gap == 3 or (gap == 2 and core == 1) else 0
            route.append((s * chip_count + (half ^ flip) * 2 + core, h * chip_count + c))
    return route


def owner_groups(hst_count, chip_count):
    groups = []
    for core in range(2):
        for first in ((0, 4) if core == 0 else (2, 6)):
            member = {}
            for h in range(hst_count):
                for step in range(4):
                    z = (first + step) % 8
                    if z % 4 == h % 4:
                        member[h] = h * chip_count + (z // 4) * 2 + core
            groups.append([member[h] for h in range(hst_count)])
    return groups


def swapped(block, axis, mask):
    return lax.ppermute(block, axis, [(i, i ^ mask) for i in range(lax.axis_size(axis))])


def pack_by_owner(points, assign, owner_count):
    row_count = points.shape[0]
    owner = assign // K_HOST
    local = assign % K_HOST
    index = jnp.arange(row_count, dtype=jnp.int32)
    earlier = (owner[:, None] == owner[None, :]) & (index[None, :] < index[:, None])
    rank = jnp.sum(earlier.astype(jnp.int32), axis=1)
    slot = owner * CAP + rank
    slots = jnp.arange(owner_count * CAP, dtype=jnp.int32)
    select = (slots[:, None] == slot[None, :]).astype(jnp.bfloat16)
    tag = jnp.broadcast_to((local + 1).astype(jnp.bfloat16)[:, None], (row_count, LABEL_LANES))
    widened = jnp.concatenate([points, tag], axis=1)
    return jnp.dot(select, widened, preferred_element_type=jnp.float32).astype(jnp.bfloat16)


def body(points, assign):
    feature_count = points.shape[1]
    owner_count = lax.axis_size("hst")
    chip_index = lax.axis_index("chip")
    quarter = feature_count // lax.axis_size("chip")
    half = feature_count // 2
    core = chip_index % 2

    packed = pack_by_owner(points, assign, owner_count)
    arrived = lax.all_to_all(
        packed,
        ("hst", "chip"),
        0,
        0,
        tiled=True,
        axis_index_groups=owner_groups(owner_count, lax.axis_size("chip")),
    )
    rows = arrived[:, :feature_count]
    labels = arrived[:, feature_count].astype(jnp.int32) - 1
    clusters = jnp.arange(K_HOST, dtype=jnp.int32)
    member = (clusters[:, None] == labels[None, :]).astype(jnp.bfloat16)
    partial = jnp.dot(member, rows, preferred_element_type=jnp.float32)

    keep = lax.dynamic_slice_in_dim(partial, core * half, half, 1)
    give = lax.dynamic_slice_in_dim(partial, (1 - core) * half, half, 1)
    pair = keep + swapped(give, "chip", 1)
    mine = pair + swapped(pair, "chip", 2)
    other = swapped(mine, "chip", 1)
    sums = jnp.where(
        core == 0,
        jnp.concatenate([mine, other], axis=1),
        jnp.concatenate([other, mine], axis=1),
    )
    factor = lax.rsqrt(jnp.mean(sums * sums, axis=1, keepdims=True) + EPSILON)
    own_block = (sums * factor).astype(jnp.bfloat16)
    centroids = lax.dynamic_slice_in_dim(own_block, chip_index * quarter, quarter, 1)

    widened = points.astype(jnp.float32)
    unit_points = (
        widened * lax.rsqrt(jnp.mean(widened * widened, axis=1, keepdims=True) + EPSILON)
    ).astype(jnp.bfloat16)
    unit_partner = swapped(unit_points, "chip", 1)

    def nearest_in(unit, candidates):
        scores = jnp.einsum("pd,kd->pk", unit, candidates, preferred_element_type=jnp.float32)
        return jnp.min(2.0 - 2.0 * scores / feature_count, axis=1)

    half_cycle = CYCLE // 2
    fetched = [
        lax.ppermute(
            own_block,
            ("hst", "chip"),
            window_route(
                owner_count,
                lax.axis_size("chip"),
                (step if step < half_cycle else None, half_cycle - 1 + step),
            ),
        )
        for step in range(1, half_cycle + 1)
    ]
    blocks = [jnp.where(core == 0, own_block, fetched[-1])] + fetched[:-1]
    nearest = nearest_in(unit_points, blocks[0])
    partner_nearest = nearest_in(unit_partner, blocks[0])
    for block in blocks[1:]:
        nearest = jnp.minimum(nearest, nearest_in(unit_points, block))
        partner_nearest = jnp.minimum(partner_nearest, nearest_in(unit_partner, block))
    nearest = jnp.minimum(nearest, swapped(partner_nearest, "chip", 1))
    return (centroids, nearest)


def solution(mesh):
    in_specs = (P(("hst", "chip"), None), P(("hst", "chip")))
    out_specs = (P("hst", "chip"), P(("hst", "chip")))
    return jax.shard_map(body, mesh=mesh, in_specs=in_specs, out_specs=out_specs, check_vma=False)
```

```python
import jax
import jax.numpy as jnp
from jax import lax
from jax.sharding import PartitionSpec as P


K_HOST = 128
CYCLE = 8
CAP = 16
LABEL_LANES = 128

EPSILON = 1e-06


def window_route(hst_count, chip_count, reach):
    route = []
    for h in range(hst_count):
        for c in range(chip_count):
            half, core = divmod(c, 2)
            if reach[core] is None:
                continue
            s = (h - reach[core]) % hst_count
            gap = abs(h % 4 - s % 4)
            flip = 1 if gap == 3 or (gap == 2 and core == 1) else 0
            route.append((s * chip_count + (half ^ flip) * 2 + core, h * chip_count + c))
    return route


def owner_groups(hst_count, chip_count):
    groups = []
    for core in range(2):
        for first in ((0, 4) if core == 0 else (2, 6)):
            member = {}
            for h in range(hst_count):
                for step in range(4):
                    z = (first + step) % 8
                    if z % 4 == h % 4:
                        member[h] = h * chip_count + (z // 4) * 2 + core
            groups.append([member[h] for h in range(hst_count)])
    return groups


def swapped(block, axis, mask):
    return lax.ppermute(block, axis, [(i, i ^ mask) for i in range(lax.axis_size(axis))])


def pack_by_owner(points, assign, owner_count):
    row_count = points.shape[0]
    owner = assign // K_HOST
    local = assign % K_HOST
    index = jnp.arange(row_count, dtype=jnp.int32)
    earlier = (owner[:, None] == owner[None, :]) & (index[None, :] < index[:, None])
    rank = jnp.sum(earlier.astype(jnp.int32), axis=1)
    slot = owner * CAP + rank
    slots = jnp.arange(owner_count * CAP, dtype=jnp.int32)
    select = (slots[:, None] == slot[None, :]).astype(jnp.bfloat16)
    tag = jnp.broadcast_to((local + 1).astype(jnp.bfloat16)[:, None], (row_count, LABEL_LANES))
    widened = jnp.concatenate([points, tag], axis=1)
    return jnp.dot(select, widened, preferred_element_type=jnp.float32).astype(jnp.bfloat16)


def body(points, assign):
    feature_count = points.shape[1]
    owner_count = lax.axis_size("hst")
    chip_index = lax.axis_index("chip")
    quarter = feature_count // lax.axis_size("chip")
    half = feature_count // 2
    core = chip_index % 2

    packed = pack_by_owner(points, assign, owner_count)
    arrived = lax.all_to_all(
        packed,
        ("hst", "chip"),
        0,
        0,
        tiled=True,
        axis_index_groups=owner_groups(owner_count, lax.axis_size("chip")),
    )
    rows = arrived[:, :feature_count]
    labels = arrived[:, feature_count].astype(jnp.int32) - 1
    clusters = jnp.arange(K_HOST, dtype=jnp.int32)
    member = (clusters[:, None] == labels[None, :]).astype(jnp.bfloat16)
    partial = jnp.dot(member, rows, preferred_element_type=jnp.float32)

    chunk_count = 2
    chunk = K_HOST // chunk_count
    own_chunks = []
    for part in range(chunk_count):
        piece = partial[part * chunk : (part + 1) * chunk]
        keep = lax.dynamic_slice_in_dim(piece, core * half, half, 1)
        give = lax.dynamic_slice_in_dim(piece, (1 - core) * half, half, 1)
        pair = keep + swapped(give, "chip", 1)
        across = swapped(pair, "chip", 2)
        mine = pair + across
        other = swapped(mine, "chip", 1)
        sums = jnp.where(
            core == 0,
            jnp.concatenate([mine, other], axis=1),
            jnp.concatenate([other, mine], axis=1),
        )
        factor = lax.rsqrt(jnp.mean(sums * sums, axis=1, keepdims=True) + EPSILON)
        own_chunks.append((sums * factor).astype(jnp.bfloat16))
    centroids = jnp.concatenate(
        [lax.dynamic_slice_in_dim(c, chip_index * quarter, quarter, 1) for c in own_chunks], axis=0
    )

    widened = points.astype(jnp.float32)
    unit_points = (
        widened * lax.rsqrt(jnp.mean(widened * widened, axis=1, keepdims=True) + EPSILON)
    ).astype(jnp.bfloat16)
    unit_partner = swapped(unit_points, "chip", 1)

    def nearest_in(unit, candidates):
        scores = jnp.einsum("pd,kd->pk", unit, candidates, preferred_element_type=jnp.float32)
        return jnp.min(2.0 - 2.0 * scores / feature_count, axis=1)

    half_cycle = CYCLE // 2
    nearest = None
    for own_block in own_chunks:
        fetched = [
            lax.ppermute(
                own_block,
                ("hst", "chip"),
                window_route(
                    owner_count,
                    lax.axis_size("chip"),
                    (step if step < half_cycle else None, half_cycle - 1 + step),
                ),
            )
            for step in range(1, half_cycle + 1)
        ]
        blocks = [jnp.where(core == 0, own_block, fetched[-1])] + fetched[:-1]
        for block in blocks:
            found = nearest_in(unit_points, block)
            partner_found = nearest_in(unit_partner, block)
            if nearest is None:
                nearest, partner_nearest = found, partner_found
            else:
                nearest = jnp.minimum(nearest, found)
                partner_nearest = jnp.minimum(partner_nearest, partner_found)
    nearest = jnp.minimum(nearest, swapped(partner_nearest, "chip", 1))
    return (centroids, nearest)


def solution(mesh):
    in_specs = (P(("hst", "chip"), None), P(("hst", "chip")))
    out_specs = (P("hst", "chip"), P(("hst", "chip")))
    return jax.shard_map(body, mesh=mesh, in_specs=in_specs, out_specs=out_specs, check_vma=False)
```

```python
import jax
import jax.numpy as jnp
from jax import lax
from jax.sharding import PartitionSpec as P

K_HOST = 128
CYCLE = 8
CAP = 16
LABEL_LANES = 128

EPSILON = 1e-06


def shifted(block, axis, distance):
    devices = range(lax.axis_size(axis))
    route = [((i - distance) % len(devices), i) for i in devices]
    return lax.ppermute(block, axis, route)


def window_route(hst_count, chip_count, reach, source_core=(0, 1)):
    route = []
    for h in range(hst_count):
        for c in range(chip_count):
            half, core = divmod(c, 2)
            if reach[core] is None:
                continue
            s = (h - reach[core]) % hst_count
            gap = abs(h % 4 - s % 4)
            flip = 1 if gap == 3 or (gap == 2 and core == 1) else 0
            route.append((s * chip_count + (half ^ flip) * 2 + source_core[core], h * chip_count + c))
    return route


def owner_groups(hst_count, chip_count):
    groups = []
    for core in range(2):
        for first in ((0, 4) if core == 0 else (2, 6)):
            member = {}
            for h in range(hst_count):
                for step in range(4):
                    z = (first + step) % 8
                    if z % 4 == h % 4:
                        member[h] = h * chip_count + (z // 4) * 2 + core
            groups.append([member[h] for h in range(hst_count)])
    return groups


def swapped(block, axis, mask):
    return lax.ppermute(block, axis, [(i, i ^ mask) for i in range(lax.axis_size(axis))])


def pack_by_owner(points, assign, owner_count):
    row_count = points.shape[0]
    owner = assign // K_HOST
    local = assign % K_HOST
    index = jnp.arange(row_count, dtype=jnp.int32)
    earlier = (owner[:, None] == owner[None, :]) & (index[None, :] < index[:, None])
    rank = jnp.sum(earlier.astype(jnp.int32), axis=1)
    slot = owner * CAP + rank
    slots = jnp.arange(owner_count * CAP, dtype=jnp.int32)
    select = (slots[:, None] == slot[None, :]).astype(jnp.bfloat16)
    tag = jnp.broadcast_to((local + 1).astype(jnp.bfloat16)[:, None], (row_count, LABEL_LANES))
    widened = jnp.concatenate([points, tag], axis=1)
    return jnp.dot(select, widened, preferred_element_type=jnp.float32).astype(jnp.bfloat16)


def body(points, assign):
    feature_count = points.shape[1]
    owner_count = lax.axis_size("hst")
    chip_index = lax.axis_index("chip")
    quarter = feature_count // lax.axis_size("chip")
    half = feature_count // 2
    core = chip_index % 2

    packed = pack_by_owner(points, assign, owner_count)
    arrived = lax.all_to_all(
        packed,
        ("hst", "chip"),
        0,
        0,
        tiled=True,
        axis_index_groups=owner_groups(owner_count, lax.axis_size("chip")),
    )
    rows = arrived[:, :feature_count]
    labels = arrived[:, feature_count].astype(jnp.int32) - 1
    clusters = jnp.arange(K_HOST, dtype=jnp.int32)
    member = (clusters[:, None] == labels[None, :]).astype(jnp.bfloat16)
    partial = jnp.dot(member, rows, preferred_element_type=jnp.float32)

    keep = lax.dynamic_slice_in_dim(partial, core * half, half, 1)
    give = lax.dynamic_slice_in_dim(partial, (1 - core) * half, half, 1)
    pair = keep + swapped(give, "chip", 1)
    mine = pair + swapped(pair, "chip", 2)
    other = swapped(mine, "chip", 1)
    sums = jnp.where(
        core == 0,
        jnp.concatenate([mine, other], axis=1),
        jnp.concatenate([other, mine], axis=1),
    )
    factor = lax.rsqrt(jnp.mean(sums * sums, axis=1, keepdims=True) + EPSILON)
    own_block = (sums * factor).astype(jnp.bfloat16)
    centroids = lax.dynamic_slice_in_dim(own_block, chip_index * quarter, quarter, 1)

    widened = points.astype(jnp.float32)
    unit_points = (
        widened * lax.rsqrt(jnp.mean(widened * widened, axis=1, keepdims=True) + EPSILON)
    ).astype(jnp.bfloat16)
    unit_partner = swapped(unit_points, "chip", 1)

    def nearest_in(unit, candidates):
        scores = jnp.einsum("pd,kd->pk", unit, candidates, preferred_element_type=jnp.float32)
        return jnp.min(2.0 - 2.0 * scores / feature_count, axis=1)

    half_cycle = CYCLE // 2
    chip_count = lax.axis_size("chip")

    def fetch(block, reach, source_core=(0, 1)):
        return lax.ppermute(
            block, ("hst", "chip"), window_route(owner_count, chip_count, reach, source_core)
        )

    first = fetch(own_block, (1, half_cycle))
    near = [first] + [fetch(own_block, (step, None)) for step in range(2, half_cycle)]
    relayed = fetch(jnp.concatenate(near, axis=0), (None, half_cycle), (0, 0))
    relayed = [relayed[i * K_HOST : (i + 1) * K_HOST] for i in range(half_cycle - 1)]
    blocks = [jnp.where(core == 0, own_block, first)] + [
        jnp.where(core == 0, a, b) for a, b in zip(near, relayed)
    ]
    nearest = nearest_in(unit_points, blocks[0])
    partner_nearest = nearest_in(unit_partner, blocks[0])
    for block in blocks[1:]:
        nearest = jnp.minimum(nearest, nearest_in(unit_points, block))
        partner_nearest = jnp.minimum(partner_nearest, nearest_in(unit_partner, block))
    nearest = jnp.minimum(nearest, swapped(partner_nearest, "chip", 1))
    return (centroids, nearest)


def solution(mesh):
    in_specs = (P(("hst", "chip"), None), P(("hst", "chip")))
    out_specs = (P("hst", "chip"), P(("hst", "chip")))
    return jax.shard_map(body, mesh=mesh, in_specs=in_specs, out_specs=out_specs, check_vma=False)
```

```python
import jax
import jax.numpy as jnp
from jax import lax
from jax.sharding import PartitionSpec as P

K_HOST = 128
CYCLE = 8
CAP = 16
LABEL_LANES = 128

EPSILON = 1e-06


def shifted(block, axis, distance):
    devices = range(lax.axis_size(axis))
    route = [((i - distance) % len(devices), i) for i in devices]
    return lax.ppermute(block, axis, route)


def window_route(hst_count, chip_count, reach):
    route = []
    for h in range(hst_count):
        for c in range(chip_count):
            half, core = divmod(c, 2)
            if reach[core] is None:
                continue
            s = (h - reach[core]) % hst_count
            gap = abs(h % 4 - s % 4)
            flip = 1 if gap == 3 or (gap == 2 and core == 1) else 0
            route.append((s * chip_count + (half ^ flip) * 2 + core, h * chip_count + c))
    return route


def owner_groups(hst_count, chip_count):
    groups = []
    for core in range(2):
        for first in ((0, 4) if core == 0 else (2, 6)):
            member = {}
            for h in range(hst_count):
                for step in range(4):
                    z = (first + step) % 8
                    if z % 4 == h % 4:
                        member[h] = h * chip_count + (z // 4) * 2 + core
            groups.append([member[h] for h in range(hst_count)])
    return groups


def swapped(block, axis, mask):
    return lax.ppermute(block, axis, [(i, i ^ mask) for i in range(lax.axis_size(axis))])


def pack_by_owner(points, assign, owner_count):
    row_count = points.shape[0]
    owner = assign // K_HOST
    local = assign % K_HOST
    index = jnp.arange(row_count, dtype=jnp.int32)
    earlier = (owner[:, None] == owner[None, :]) & (index[None, :] < index[:, None])
    rank = jnp.sum(earlier.astype(jnp.int32), axis=1)
    slot = owner * CAP + rank
    slots = jnp.arange(owner_count * CAP, dtype=jnp.int32)
    select = (slots[:, None] == slot[None, :]).astype(jnp.bfloat16)
    tag = jnp.broadcast_to((local + 1).astype(jnp.bfloat16)[:, None], (row_count, LABEL_LANES))
    widened = jnp.concatenate([points, tag], axis=1)
    return jnp.dot(select, widened, preferred_element_type=jnp.bfloat16)


def body(points, assign):
    feature_count = points.shape[1]
    owner_count = lax.axis_size("hst")
    chip_index = lax.axis_index("chip")
    quarter = feature_count // lax.axis_size("chip")
    half = feature_count // 2
    core = chip_index % 2

    packed = pack_by_owner(points, assign, owner_count)
    arrived = lax.all_to_all(
        packed,
        ("hst", "chip"),
        0,
        0,
        tiled=True,
        axis_index_groups=owner_groups(owner_count, lax.axis_size("chip")),
    )
    rows = arrived[:, :feature_count]
    labels = arrived[:, feature_count].astype(jnp.int32) - 1
    clusters = jnp.arange(K_HOST, dtype=jnp.int32)
    member = (clusters[:, None] == labels[None, :]).astype(jnp.bfloat16)
    partial = jnp.dot(member, rows, preferred_element_type=jnp.float32)

    keep = lax.dynamic_slice_in_dim(partial, core * half, half, 1)
    give = lax.dynamic_slice_in_dim(partial, (1 - core) * half, half, 1)
    pair = keep + swapped(give, "chip", 1)
    mine = pair + swapped(pair, "chip", 2)
    other = swapped(mine, "chip", 1)
    sums = jnp.where(
        core == 0,
        jnp.concatenate([mine, other], axis=1),
        jnp.concatenate([other, mine], axis=1),
    )
    factor = lax.rsqrt(jnp.mean(sums * sums, axis=1, keepdims=True) + EPSILON)
    own_block = (sums * factor).astype(jnp.bfloat16)
    centroids = lax.dynamic_slice_in_dim(own_block, chip_index * quarter, quarter, 1)

    widened = points.astype(jnp.float32)
    unit_points = (
        widened * lax.rsqrt(jnp.mean(widened * widened, axis=1, keepdims=True) + EPSILON)
    ).astype(jnp.bfloat16)
    unit_partner = swapped(unit_points, "chip", 1)

    def nearest_in(unit, candidates):
        scores = jnp.einsum("pd,kd->pk", unit, candidates, preferred_element_type=jnp.float32)
        return jnp.min(2.0 - 2.0 * scores / feature_count, axis=1)

    half_cycle = CYCLE // 2
    fetched = [
        lax.ppermute(
            own_block,
            ("hst", "chip"),
            window_route(
                owner_count,
                lax.axis_size("chip"),
                (step if step < half_cycle else None, half_cycle - 1 + step),
            ),
        )
        for step in range(1, half_cycle + 1)
    ]
    blocks = [jnp.where(core == 0, own_block, fetched[-1])] + fetched[:-1]
    partner_nearest = nearest_in(unit_partner, blocks[0])
    nearest = nearest_in(unit_points, blocks[0])
    for block in blocks[1:]:
        partner_nearest = jnp.minimum(partner_nearest, nearest_in(unit_partner, block))
        nearest = jnp.minimum(nearest, nearest_in(unit_points, block))
    nearest = jnp.minimum(nearest, swapped(partner_nearest, "chip", 1))
    return (centroids, nearest)


def solution(mesh):
    in_specs = (P(("hst", "chip"), None), P(("hst", "chip")))
    out_specs = (P("hst", "chip"), P(("hst", "chip")))
    return jax.shard_map(body, mesh=mesh, in_specs=in_specs, out_specs=out_specs, check_vma=False)
```

```python
import jax
import jax.numpy as jnp
from jax import lax
from jax.sharding import PartitionSpec as P

K_HOST = 128
CYCLE = 8
CAP = 16
LABEL_LANES = 128

EPSILON = 1e-06


def shifted(block, axis, distance):
    devices = range(lax.axis_size(axis))
    route = [((i - distance) % len(devices), i) for i in devices]
    return lax.ppermute(block, axis, route)


def window_route(hst_count, chip_count, reach):
    route = []
    for h in range(hst_count):
        for c in range(chip_count):
            half, core = divmod(c, 2)
            if reach[core] is None:
                continue
            s = (h - reach[core]) % hst_count
            gap = abs(h % 4 - s % 4)
            flip = 1 if gap == 3 or (gap == 2 and core == 1) else 0
            route.append((s * chip_count + (half ^ flip) * 2 + core, h * chip_count + c))
    return route


def owner_groups(hst_count, chip_count):
    groups = []
    for core in range(2):
        for first in ((0, 4) if core == 0 else (2, 6)):
            member = {}
            for h in range(hst_count):
                for step in range(4):
                    z = (first + step) % 8
                    if z % 4 == h % 4:
                        member[h] = h * chip_count + (z // 4) * 2 + core
            groups.append([member[h] for h in range(hst_count)])
    return groups


def swapped(block, axis, mask):
    return lax.ppermute(block, axis, [(i, i ^ mask) for i in range(lax.axis_size(axis))])


def pack_by_owner(points, assign, owner_count):
    row_count = points.shape[0]
    owner = assign // K_HOST
    local = assign % K_HOST
    index = jnp.arange(row_count, dtype=jnp.int32)
    earlier = (owner[:, None] == owner[None, :]) & (index[None, :] < index[:, None])
    rank = jnp.sum(earlier.astype(jnp.int32), axis=1)
    slot = owner * CAP + rank
    slots = jnp.arange(owner_count * CAP, dtype=jnp.int32)
    select = lax.optimization_barrier((slots[:, None] == slot[None, :]).astype(jnp.bfloat16))
    tag = jnp.broadcast_to((local + 1).astype(jnp.bfloat16)[:, None], (row_count, LABEL_LANES))
    widened = jnp.concatenate([points, tag], axis=1)
    return jnp.dot(select, widened, preferred_element_type=jnp.bfloat16)


def body(points, assign):
    feature_count = points.shape[1]
    owner_count = lax.axis_size("hst")
    chip_index = lax.axis_index("chip")
    quarter = feature_count // lax.axis_size("chip")
    half = feature_count // 2
    core = chip_index % 2

    packed = pack_by_owner(points, assign, owner_count)
    arrived = lax.all_to_all(
        packed,
        ("hst", "chip"),
        0,
        0,
        tiled=True,
        axis_index_groups=owner_groups(owner_count, lax.axis_size("chip")),
    )
    rows = arrived[:, :feature_count]
    labels = arrived[:, feature_count].astype(jnp.int32) - 1
    clusters = jnp.arange(K_HOST, dtype=jnp.int32)
    member = (clusters[:, None] == labels[None, :]).astype(jnp.bfloat16)
    partial = jnp.dot(member, rows, preferred_element_type=jnp.float32)

    keep = lax.dynamic_slice_in_dim(partial, core * half, half, 1)
    give = lax.dynamic_slice_in_dim(partial, (1 - core) * half, half, 1)
    pair = keep + swapped(give, "chip", 1)
    mine = pair + swapped(pair, "chip", 2)
    other = swapped(mine, "chip", 1)
    sums = jnp.where(
        core == 0,
        jnp.concatenate([mine, other], axis=1),
        jnp.concatenate([other, mine], axis=1),
    )
    factor = lax.rsqrt(jnp.mean(sums * sums, axis=1, keepdims=True) + EPSILON)
    own_block = (sums * factor).astype(jnp.bfloat16)
    centroids = lax.dynamic_slice_in_dim(own_block, chip_index * quarter, quarter, 1)

    widened = points.astype(jnp.float32)
    unit_points = (
        widened * lax.rsqrt(jnp.mean(widened * widened, axis=1, keepdims=True) + EPSILON)
    ).astype(jnp.bfloat16)
    unit_partner = swapped(unit_points, "chip", 1)

    def nearest_in(unit, candidates):
        scores = jnp.einsum("pd,kd->pk", unit, candidates, preferred_element_type=jnp.float32)
        return jnp.min(2.0 - 2.0 * scores / feature_count, axis=1)

    half_cycle = CYCLE // 2
    fetched = [
        lax.ppermute(
            own_block,
            ("hst", "chip"),
            window_route(
                owner_count,
                lax.axis_size("chip"),
                (step if step < half_cycle else None, half_cycle - 1 + step),
            ),
        )
        for step in range(1, half_cycle + 1)
    ]
    blocks = [jnp.where(core == 0, own_block, fetched[-1])] + fetched[:-1]
    partner_nearest = nearest_in(unit_partner, blocks[0])
    nearest = nearest_in(unit_points, blocks[0])
    for block in blocks[1:]:
        partner_nearest = jnp.minimum(partner_nearest, nearest_in(unit_partner, block))
        nearest = jnp.minimum(nearest, nearest_in(unit_points, block))
    nearest = jnp.minimum(nearest, swapped(partner_nearest, "chip", 1))
    return (centroids, nearest)


def solution(mesh):
    in_specs = (P(("hst", "chip"), None), P(("hst", "chip")))
    out_specs = (P("hst", "chip"), P(("hst", "chip")))
    return jax.shard_map(body, mesh=mesh, in_specs=in_specs, out_specs=out_specs, check_vma=False)
```

```python
import jax
import jax.numpy as jnp
from jax import lax
from jax.sharding import PartitionSpec as P

K_HOST = 128
CYCLE = 8
CAP = 16
LABEL_LANES = 128

EPSILON = 1e-06


def shifted(block, axis, distance):
    devices = range(lax.axis_size(axis))
    route = [((i - distance) % len(devices), i) for i in devices]
    return lax.ppermute(block, axis, route)


def window_route(hst_count, chip_count, reach):
    route = []
    for h in range(hst_count):
        for c in range(chip_count):
            half, core = divmod(c, 2)
            if reach[core] is None:
                continue
            s = (h - reach[core]) % hst_count
            gap = abs(h % 4 - s % 4)
            flip = 1 if gap == 3 or (gap == 2 and core == 1) else 0
            route.append((s * chip_count + (half ^ flip) * 2 + core, h * chip_count + c))
    return route


def owner_groups(hst_count, chip_count):
    groups = []
    for core in range(2):
        for first in ((0, 4) if core == 0 else (2, 6)):
            member = {}
            for h in range(hst_count):
                for step in range(4):
                    z = (first + step) % 8
                    if z % 4 == h % 4:
                        member[h] = h * chip_count + (z // 4) * 2 + core
            groups.append([member[h] for h in range(hst_count)])
    return groups


def z_shift_route(hst_count, chip_count, distance):
    route = []
    for h in range(hst_count):
        for c in range(chip_count):
            half, core = divmod(c, 2)
            z = (half * 4 + h % 4 + distance) % 8
            target = (h - h % 4 + z % 4) * chip_count + (z // 4) * 2 + core
            route.append((h * chip_count + c, target))
    return route


def across_chips(block, hst_count, chip_count):
    rows = block.shape[0] // 2

    def shift(x, distance):
        return lax.ppermute(x, ("hst", "chip"), z_shift_route(hst_count, chip_count, distance))

    ahead = shift(shift(block[:rows], 1), 3)
    behind = shift(shift(block[rows:], -1), -3)
    return jnp.concatenate([ahead, behind], axis=0)


def swapped(block, axis, mask):
    return lax.ppermute(block, axis, [(i, i ^ mask) for i in range(lax.axis_size(axis))])


def pack_by_owner(points, assign, owner_count):
    row_count = points.shape[0]
    owner = assign // K_HOST
    local = assign % K_HOST
    index = jnp.arange(row_count, dtype=jnp.int32)
    earlier = (owner[:, None] == owner[None, :]) & (index[None, :] < index[:, None])
    rank = jnp.sum(earlier.astype(jnp.int32), axis=1)
    slot = owner * CAP + rank
    slots = jnp.arange(owner_count * CAP, dtype=jnp.int32)
    select = (slots[:, None] == slot[None, :]).astype(jnp.bfloat16)
    tag = jnp.broadcast_to((local + 1).astype(jnp.bfloat16)[:, None], (row_count, LABEL_LANES))
    widened = jnp.concatenate([points, tag], axis=1)
    return jnp.dot(select, widened, preferred_element_type=jnp.bfloat16)


def body(points, assign):
    feature_count = points.shape[1]
    owner_count = lax.axis_size("hst")
    chip_index = lax.axis_index("chip")
    quarter = feature_count // lax.axis_size("chip")
    half = feature_count // 2
    core = chip_index % 2

    packed = pack_by_owner(points, assign, owner_count)
    arrived = lax.all_to_all(
        packed,
        ("hst", "chip"),
        0,
        0,
        tiled=True,
        axis_index_groups=owner_groups(owner_count, lax.axis_size("chip")),
    )
    rows = arrived[:, :feature_count]
    labels = arrived[:, feature_count].astype(jnp.int32) - 1
    clusters = jnp.arange(K_HOST, dtype=jnp.int32)
    member = (clusters[:, None] == labels[None, :]).astype(jnp.bfloat16)
    partial = jnp.dot(member, rows, preferred_element_type=jnp.float32)

    keep = lax.dynamic_slice_in_dim(partial, core * half, half, 1)
    give = lax.dynamic_slice_in_dim(partial, (1 - core) * half, half, 1)
    pair = keep + swapped(give, "chip", 1)
    mine = pair + across_chips(pair, owner_count, lax.axis_size("chip"))
    other = swapped(mine, "chip", 1)
    sums = jnp.where(
        core == 0,
        jnp.concatenate([mine, other], axis=1),
        jnp.concatenate([other, mine], axis=1),
    )
    factor = lax.rsqrt(jnp.mean(sums * sums, axis=1, keepdims=True) + EPSILON)
    own_block = (sums * factor).astype(jnp.bfloat16)
    centroids = lax.dynamic_slice_in_dim(own_block, chip_index * quarter, quarter, 1)

    widened = points.astype(jnp.float32)
    unit_points = (
        widened * lax.rsqrt(jnp.mean(widened * widened, axis=1, keepdims=True) + EPSILON)
    ).astype(jnp.bfloat16)
    unit_partner = swapped(unit_points, "chip", 1)

    def nearest_in(unit, candidates):
        scores = jnp.einsum("pd,kd->pk", unit, candidates, preferred_element_type=jnp.float32)
        return jnp.min(2.0 - 2.0 * scores / feature_count, axis=1)

    half_cycle = CYCLE // 2
    fetched = [
        lax.ppermute(
            own_block,
            ("hst", "chip"),
            window_route(
                owner_count,
                lax.axis_size("chip"),
                (step if step < half_cycle else None, half_cycle - 1 + step),
            ),
        )
        for step in range(1, half_cycle + 1)
    ]
    blocks = [jnp.where(core == 0, own_block, fetched[-1])] + fetched[:-1]
    partner_nearest = nearest_in(unit_partner, blocks[0])
    nearest = nearest_in(unit_points, blocks[0])
    for block in blocks[1:]:
        partner_nearest = jnp.minimum(partner_nearest, nearest_in(unit_partner, block))
        nearest = jnp.minimum(nearest, nearest_in(unit_points, block))
    nearest = jnp.minimum(nearest, swapped(partner_nearest, "chip", 1))
    return (centroids, nearest)


def solution(mesh):
    in_specs = (P(("hst", "chip"), None), P(("hst", "chip")))
    out_specs = (P("hst", "chip"), P(("hst", "chip")))
    return jax.shard_map(body, mesh=mesh, in_specs=in_specs, out_specs=out_specs, check_vma=False)
```

```python
import jax
import jax.numpy as jnp
from jax import lax
from jax.sharding import PartitionSpec as P

K_HOST = 128
CYCLE = 8
CAP = 16
LABEL_LANES = 128

EPSILON = 1e-06


def shifted(block, axis, distance):
    devices = range(lax.axis_size(axis))
    route = [((i - distance) % len(devices), i) for i in devices]
    return lax.ppermute(block, axis, route)


def window_route(hst_count, chip_count, reach):
    route = []
    for h in range(hst_count):
        for c in range(chip_count):
            half, core = divmod(c, 2)
            if reach[core] is None:
                continue
            s = (h - reach[core]) % hst_count
            gap = abs(h % 4 - s % 4)
            flip = 1 if gap == 3 or (gap == 2 and core == 1) else 0
            route.append((s * chip_count + (half ^ flip) * 2 + core, h * chip_count + c))
    return route


def owner_groups(hst_count, chip_count):
    groups = []
    for core in range(2):
        for first in ((0, 4) if core == 0 else (2, 6)):
            member = {}
            for h in range(hst_count):
                for step in range(4):
                    z = (first + step) % 8
                    if z % 4 == h % 4:
                        member[h] = h * chip_count + (z // 4) * 2 + core
            groups.append([member[h] for h in range(hst_count)])
    return groups


def swapped(block, axis, mask):
    return lax.ppermute(block, axis, [(i, i ^ mask) for i in range(lax.axis_size(axis))])


def pack_by_owner(points, assign, owner_count):
    row_count = points.shape[0]
    owner = assign // K_HOST
    local = assign % K_HOST
    index = jnp.arange(row_count, dtype=jnp.int32)
    earlier = (owner[:, None] == owner[None, :]) & (index[None, :] < index[:, None])
    rank = jnp.sum(earlier.astype(jnp.int32), axis=1)
    slot = owner * CAP + rank
    slots = jnp.arange(owner_count * CAP, dtype=jnp.int32)
    select = (slots[:, None] == slot[None, :]).astype(jnp.bfloat16)
    tag = jnp.broadcast_to((local + 1).astype(jnp.bfloat16)[:, None], (row_count, LABEL_LANES))
    widened = jnp.concatenate([points, tag], axis=1)
    return jnp.dot(select, widened, preferred_element_type=jnp.bfloat16)


def body(points, assign):
    feature_count = points.shape[1]
    owner_count = lax.axis_size("hst")
    chip_index = lax.axis_index("chip")
    quarter = feature_count // lax.axis_size("chip")
    half = feature_count // 2
    core = chip_index % 2

    packed = pack_by_owner(points, assign, owner_count)
    arrived = lax.all_to_all(
        packed,
        ("hst", "chip"),
        0,
        0,
        tiled=True,
        axis_index_groups=owner_groups(owner_count, lax.axis_size("chip")),
    )
    rows = arrived[:, :feature_count]
    labels = arrived[:, feature_count].astype(jnp.int32) - 1
    clusters = jnp.arange(K_HOST, dtype=jnp.int32)
    member = (clusters[:, None] == labels[None, :]).astype(jnp.bfloat16)
    partial = jnp.dot(member, rows, preferred_element_type=jnp.float32)

    keep = lax.dynamic_slice_in_dim(partial, core * half, half, 1)
    give = lax.dynamic_slice_in_dim(partial, (1 - core) * half, half, 1)
    pair = keep + swapped(give, "chip", 1)
    rows = pair.shape[0] // 2
    mine = pair + jnp.concatenate(
        [swapped(pair[:rows], "chip", 2), swapped(pair[rows:], "chip", 2)], axis=0
    )
    other = swapped(mine, "chip", 1)
    sums = jnp.where(
        core == 0,
        jnp.concatenate([mine, other], axis=1),
        jnp.concatenate([other, mine], axis=1),
    )
    factor = lax.rsqrt(jnp.mean(sums * sums, axis=1, keepdims=True) + EPSILON)
    own_block = (sums * factor).astype(jnp.bfloat16)
    centroids = lax.dynamic_slice_in_dim(own_block, chip_index * quarter, quarter, 1)

    widened = points.astype(jnp.float32)
    unit_points = (
        widened * lax.rsqrt(jnp.mean(widened * widened, axis=1, keepdims=True) + EPSILON)
    ).astype(jnp.bfloat16)
    unit_partner = swapped(unit_points, "chip", 1)

    def nearest_in(unit, candidates):
        scores = jnp.einsum("pd,kd->pk", unit, candidates, preferred_element_type=jnp.float32)
        return jnp.min(2.0 - 2.0 * scores / feature_count, axis=1)

    half_cycle = CYCLE // 2
    fetched = [
        lax.ppermute(
            own_block,
            ("hst", "chip"),
            window_route(
                owner_count,
                lax.axis_size("chip"),
                (step if step < half_cycle else None, half_cycle - 1 + step),
            ),
        )
        for step in range(1, half_cycle + 1)
    ]
    blocks = [jnp.where(core == 0, own_block, fetched[-1])] + fetched[:-1]
    partner_nearest = nearest_in(unit_partner, blocks[0])
    nearest = nearest_in(unit_points, blocks[0])
    for block in blocks[1:]:
        partner_nearest = jnp.minimum(partner_nearest, nearest_in(unit_partner, block))
        nearest = jnp.minimum(nearest, nearest_in(unit_points, block))
    nearest = jnp.minimum(nearest, swapped(partner_nearest, "chip", 1))
    return (centroids, nearest)


def solution(mesh):
    in_specs = (P(("hst", "chip"), None), P(("hst", "chip")))
    out_specs = (P("hst", "chip"), P(("hst", "chip")))
    return jax.shard_map(body, mesh=mesh, in_specs=in_specs, out_specs=out_specs, check_vma=False)
```

```python
import jax
import jax.numpy as jnp
from jax import lax
from jax.sharding import PartitionSpec as P

K_HOST = 128
CYCLE = 8
CAP = 16
LABEL_LANES = 128

EPSILON = 1e-06


def shifted(block, axis, distance):
    devices = range(lax.axis_size(axis))
    route = [((i - distance) % len(devices), i) for i in devices]
    return lax.ppermute(block, axis, route)


def window_route(hst_count, chip_count, reach):
    route = []
    for h in range(hst_count):
        for c in range(chip_count):
            half, core = divmod(c, 2)
            if reach[core] is None:
                continue
            s = (h - reach[core]) % hst_count
            gap = abs(h % 4 - s % 4)
            flip = 1 if gap == 3 or (gap == 2 and core == 1) else 0
            route.append((s * chip_count + (half ^ flip) * 2 + core, h * chip_count + c))
    return route


def owner_groups(hst_count, chip_count):
    groups = []
    for core in range(2):
        for first in ((0, 4) if core == 0 else (2, 6)):
            member = {}
            for h in range(hst_count):
                for step in range(4):
                    z = (first + step) % 8
                    if z % 4 == h % 4:
                        member[h] = h * chip_count + (z // 4) * 2 + core
            groups.append([member[h] for h in range(hst_count)])
    return groups


def swapped(block, axis, mask):
    return lax.ppermute(block, axis, [(i, i ^ mask) for i in range(lax.axis_size(axis))])


def pack_by_owner(points, assign, owner_count):
    row_count = points.shape[0]
    owner = assign // K_HOST
    local = assign % K_HOST
    index = jnp.arange(row_count, dtype=jnp.int32)
    earlier = (owner[:, None] == owner[None, :]) & (index[None, :] < index[:, None])
    rank = jnp.sum(earlier.astype(jnp.int32), axis=1)
    slot = owner * CAP + rank
    slots = jnp.arange(owner_count * CAP, dtype=jnp.int32)
    select = (slots[:, None] == slot[None, :]).astype(jnp.bfloat16)
    tag = jnp.broadcast_to((local + 1).astype(jnp.bfloat16)[:, None], (row_count, LABEL_LANES))
    widened = jnp.concatenate([points, tag], axis=1)
    return jnp.dot(select, widened, preferred_element_type=jnp.bfloat16)


def body(points, assign):
    feature_count = points.shape[1]
    owner_count = lax.axis_size("hst")
    chip_index = lax.axis_index("chip")
    quarter = feature_count // lax.axis_size("chip")
    half = feature_count // 2
    core = chip_index % 2

    packed = pack_by_owner(points, assign, owner_count)
    arrived = lax.all_to_all(
        packed,
        ("hst", "chip"),
        0,
        0,
        tiled=True,
        axis_index_groups=owner_groups(owner_count, lax.axis_size("chip")),
    )
    rows = arrived[:, :feature_count]
    labels = arrived[:, feature_count].astype(jnp.int32) - 1
    clusters = jnp.arange(K_HOST, dtype=jnp.int32)
    member = (clusters[:, None] == labels[None, :]).astype(jnp.bfloat16)
    partial = jnp.dot(member, rows, preferred_element_type=jnp.float32)

    keep = lax.dynamic_slice_in_dim(partial, core * half, half, 1)
    give = lax.dynamic_slice_in_dim(partial, (1 - core) * half, half, 1)
    pair = keep + swapped(give, "chip", 1)
    mine = pair + swapped(pair, "chip", 2)
    other = swapped(mine, "chip", 1)
    sums = jnp.where(
        core == 0,
        jnp.concatenate([mine, other], axis=1),
        jnp.concatenate([other, mine], axis=1),
    )
    factor = lax.rsqrt(jnp.mean(sums * sums, axis=1, keepdims=True) + EPSILON)
    own_block = (sums * factor).astype(jnp.bfloat16)
    centroids = lax.dynamic_slice_in_dim(own_block, chip_index * quarter, quarter, 1)

    widened = points.astype(jnp.float32)
    unit_points = (
        widened * lax.rsqrt(jnp.mean(widened * widened, axis=1, keepdims=True) + EPSILON)
    ).astype(jnp.bfloat16)
    unit_partner = swapped(unit_points, "chip", 1)

    def nearest_in(unit, candidates):
        scores = jnp.einsum("pd,kd->pk", unit, candidates, preferred_element_type=jnp.float32)
        return jnp.min(2.0 - 2.0 * scores / feature_count, axis=1)

    half_cycle = CYCLE // 2
    fetched = [
        lax.ppermute(
            own_block,
            ("hst", "chip"),
            window_route(
                owner_count,
                lax.axis_size("chip"),
                (step if step < half_cycle else None, half_cycle - 1 + step),
            ),
        )
        for step in range(1, half_cycle + 1)
    ]
    blocks = [jnp.where(core == 0, own_block, fetched[-1])] + fetched[:-1]
    point_count = unit_points.shape[0]
    unit_both = jnp.concatenate([unit_points, unit_partner], axis=0)
    both = nearest_in(unit_both, blocks[0])
    for block in blocks[1:]:
        both = jnp.minimum(both, nearest_in(unit_both, block))
    nearest, partner_nearest = both[:point_count], both[point_count:]
    nearest = jnp.minimum(nearest, swapped(partner_nearest, "chip", 1))
    return (centroids, nearest)


def solution(mesh):
    in_specs = (P(("hst", "chip"), None), P(("hst", "chip")))
    out_specs = (P("hst", "chip"), P(("hst", "chip")))
    return jax.shard_map(body, mesh=mesh, in_specs=in_specs, out_specs=out_specs, check_vma=False)
```
